32 devices in a mesh: outer: 4 (over z), inner: 8 (over y, x, core).
Axes of the slice: x: 2, y: 2, z: 4, core: 2. Of those that a mesh axis runs over, the one named last changes fastest.
Arguments:
- queries: bfloat16 [8192, 1024], P(('outer', 'inner')), may hold values from -60 to 60
- key_states: bfloat16 [8192, 128], P(('outer', 'inner')), may hold values from -6 to 6
- value_states: bfloat16 [8192, 128], P(('outer', 'inner')), may hold values from -6 to 6
- grad_output: bfloat16 [8192, 1024], P(('outer', 'inner')), may hold values from -6 to 6
- documents: int32 [8192], replicated, may hold values from 0 to 20, never falling along the last dimension, each value on 1 to 768 neighbouring positions
- block_order: int32 [64], replicated, may hold values from 0 to 63, as said below
Outputs:
- grad_queries: bfloat16 [8192, 1024], P(('outer', 'inner'))
- grad_keys: bfloat16 [8192, 128], P(('outer', 'inner'))
- grad_values: bfloat16 [8192, 128], P(('outer', 'inner'))
The draws below stay inside these ranges and needn't reach their ends.
Inputs may be any that keep to these rules, and one draw needn't show every extreme that they name: `documents`: never falling along the sequence; every document has 1 to 768 positions and one has exactly 768. `block_order`: device d of the joined index outer, inner (d = outer * 8 + inner) holds stored blocks 2 * d and 2 * d + 1, which are sequence blocks d and 63 - d in either order.
All inputs are finite; a program needn't handle non-finite values.
Results may differ from the reference program's by a relative error of at most 0.0049.
Values may be sent and summed in bfloat16 or wider, within the bound.
No kernel may reach another device: no remote copies, remote signals or barrier semaphores. Data moves between devices by JAX's collectives and lax.ppermute only.
A program may use at most 64 MiB of HBM per device.

```python
import math
import jax
import jax.numpy as jnp
import numpy as np
from jax import lax

D_HEAD = 128
HEADS = 8
REACH = 6
BLK = 128
DOC_MOST = 768
BLOCKS = 64
TOKENS = 8192


def attention_draws(key):
    base_key = jax.random.fold_in(key, 29)
    key_draw, query_draw = jax.random.split(base_key, 2)
    key_rows = jnp.clip(jax.random.normal(key_draw, (TOKENS, D_HEAD), jnp.float32), -6.0, 6.0)
    query_rows = jnp.clip(jax.random.normal(query_draw, (TOKENS, HEADS, D_HEAD), jnp.float32), -6.0, 6.0)
    return (key_rows, query_rows.reshape(TOKENS, HEADS * D_HEAD))


def draw_queries(key, part):
    return attention_draws(key)[1].astype(jnp.bfloat16)


def draw_key_states(key, part):
    return attention_draws(key)[0].astype(jnp.bfloat16)


def draw_block_order(key, part):
    half_count = BLOCKS // 2
    swapped = jax.random.randint(jax.random.fold_in(key, 7), (half_count,), 0, 2, dtype=jnp.int32)
    lower_half = jnp.arange(half_count, dtype=jnp.int32)
    upper_half = BLOCKS - 1 - lower_half
    slot_zero = jnp.where(swapped == 1, upper_half, lower_half)
    slot_one = jnp.where(swapped == 1, lower_half, upper_half)
    return jnp.stack([slot_zero, slot_one], 1).reshape(BLOCKS).astype(jnp.int32)


def levels(key, extent, shards, smallest, largest):
    level = 1.0
    for dim, parts in shards:
        steps = jax.random.uniform(jax.random.fold_in(jax.random.fold_in(key, 6), dim), (parts,), jnp.float32, smallest / len(shards), largest / len(shards))
        level = level * jnp.repeat(jnp.exp(steps), extent[dim] // parts).reshape((-1,) + (1,) * (len(extent) - 1 - dim))
    return level


def profile(amount, total, reach, lean):
    loads = [(1 << 20) // math.isqrt(rank ** lean) + 1 for rank in range(2, amount + 1)]
    rest, given = total - reach - (amount - 1), [1] * (amount - 1)
    while rest > 0:
        movable = [i for i in range(amount - 1) if given[i] < reach]
        pool, remaining = sum([loads[i] for i in movable]), rest
        for i in movable:
            addition = min(reach - given[i], max(1, remaining * loads[i] // pool), rest)
            given[i] = given[i] + addition
            rest = rest - addition
    return np.array([reach] + given)


def uneven(key, number_of, total, most, lean):
    if number_of == 2:
        one = jax.random.randint(key, (), max(1, total - most), min(most, total - 1) + 1)
        return jnp.stack([one, total - one])
    sizes = jnp.asarray(profile(number_of, total, most, lean), jnp.int32)
    twos = (number_of - 1) // 2
    source_of, sink = sizes[1:1 + 2 * twos:2], sizes[2:2 + 2 * twos:2]
    room = jnp.minimum(source_of - 1, most - sink)
    passed = jax.random.randint(jax.random.fold_in(key, 1), (twos,), 0, 1 << 20) % (room + 1)
    sizes = sizes.at[1:1 + 2 * twos:2].set(source_of - passed).at[2:2 + 2 * twos:2].set(sink + passed)
    return sizes[jax.random.permutation(jax.random.fold_in(key, 2), number_of)]


def normal_values(stream_key, shape, width, bound, shards=(), kind=jnp.bfloat16):
    array = width * jax.random.normal(stream_key, shape, jnp.float32)
    if shards:
        array = array * levels(stream_key, shape, shards, -0.22, 0.18)
    return jnp.clip(array, -bound, bound).astype(kind)


def setup_inputs(seed: int = 0) -> dict:
    streams_of = jax.random.split(jax.random.key(seed), 7)
    return {
        "queries": draw_queries(jax.random.fold_in(streams_of[6], 71), 0),
        "key_states": draw_key_states(jax.random.fold_in(streams_of[6], 71), 0),
        "value_states": normal_values(streams_of[2], (TOKENS, D_HEAD), 1.0, 6.0, ((0, 32),)),
        "grad_output": normal_values(streams_of[3], (TOKENS, HEADS * D_HEAD), 1.0, 6.0, ((0, 32),)),
        "documents": jnp.searchsorted(jnp.cumsum(uneven(streams_of[4], 2 * BLOCKS // REACH, TOKENS, DOC_MOST, 2)), jnp.arange(TOKENS), side="right").astype(jnp.int32),
        "block_order": draw_block_order(jax.random.fold_in(streams_of[6], 71), 0),
    }


NEGATIVE = -1e+30

def rounded(values):
    return lax.optimization_barrier(values.astype(jnp.bfloat16)).astype(jnp.float32)

def to_sequence(stored, block_order):
    blocks = stored.reshape(BLOCKS, BLK, stored.shape[1])
    return jnp.zeros_like(blocks).at[block_order].set(blocks).reshape(stored.shape)

def to_stored(sequence, block_order):
    blocks = sequence.reshape(BLOCKS, BLK, sequence.shape[1])
    return blocks[block_order].reshape(sequence.shape)

def reference(queries, key_states, value_states, grad_output, documents, block_order):
    factor = 1.0 / math.sqrt(D_HEAD)
    pad_rows = REACH * BLK
    window_rows = (REACH + 1) * BLK
    ordered_queries = to_sequence(queries, block_order).reshape(TOKENS, HEADS, D_HEAD)
    ordered_outputs = to_sequence(grad_output, block_order).reshape(TOKENS, HEADS, D_HEAD)
    ordered_keys = to_sequence(key_states, block_order)
    ordered_values = to_sequence(value_states, block_order)
    early_keys = jnp.concatenate([jnp.zeros((pad_rows, D_HEAD), ordered_keys.dtype), ordered_keys], 0)
    early_values = jnp.concatenate([jnp.zeros((pad_rows, D_HEAD), ordered_values.dtype), ordered_values], 0)
    early_owner = jnp.concatenate([jnp.full((pad_rows,), -1, jnp.int32), documents], 0)
    block_offsets = jnp.arange(BLK, dtype=jnp.int32)
    window_offsets = jnp.arange(window_rows, dtype=jnp.int32)

    def query_block(block_index):
        row_start = (block_index * BLK).astype(jnp.int32)
        query_rows = lax.dynamic_slice_in_dim(ordered_queries, row_start, BLK, 0).astype(jnp.float32)
        output_rows = lax.dynamic_slice_in_dim(ordered_outputs, row_start, BLK, 0).astype(jnp.float32)
        key_window = lax.dynamic_slice_in_dim(early_keys, row_start, window_rows, 0).astype(jnp.float32)
        value_window = lax.dynamic_slice_in_dim(early_values, row_start, window_rows, 0).astype(jnp.float32)
        query_owner = lax.dynamic_slice_in_dim(documents, row_start, BLK, 0)
        key_owner = lax.dynamic_slice_in_dim(early_owner, row_start, window_rows, 0)
        query_place = row_start + block_offsets
        key_place = row_start - pad_rows + window_offsets
        allowed = (key_place[None, :] <= query_place[:, None]) & (key_place[None, :] >= 0) & (key_owner[None, :] == query_owner[:, None])
        scores = jnp.einsum('bhd,wd->hbw', query_rows, key_window) * factor
        grad_prob = jnp.einsum('bhd,wd->hbw', output_rows, value_window)
        masked = jnp.where(allowed[None], scores, NEGATIVE)
        top_score = masked.max(-1)
        weights = jnp.where(allowed[None], jnp.exp(scores - top_score[..., None]), 0.0)
        log_totals = top_score + jnp.log(weights.sum(-1))
        probabilities = jnp.where(allowed[None], jnp.exp(scores - log_totals[..., None]), 0.0)
        row_dots = (probabilities * grad_prob).sum(-1)
        grad_scores = rounded(probabilities * (grad_prob - row_dots[..., None]))
        grad_rows = jnp.einsum('hbw,wd->bhd', grad_scores, key_window) * factor
        return (grad_rows.astype(jnp.bfloat16).reshape(BLK, HEADS * D_HEAD), log_totals.T, row_dots.T)
    grad_blocks, total_blocks, dot_blocks = lax.map(query_block, jnp.arange(BLOCKS, dtype=jnp.int32))
    grad_query_rows = grad_blocks.reshape(TOKENS, HEADS * D_HEAD)
    log_all = total_blocks.reshape(TOKENS, HEADS)
    dots_all = dot_blocks.reshape(TOKENS, HEADS)
    late_queries = jnp.concatenate([ordered_queries, jnp.zeros((pad_rows, HEADS, D_HEAD), ordered_queries.dtype)], 0)
    late_outputs = jnp.concatenate([ordered_outputs, jnp.zeros((pad_rows, HEADS, D_HEAD), ordered_outputs.dtype)], 0)
    late_totals = jnp.concatenate([log_all, jnp.zeros((pad_rows, HEADS), log_all.dtype)], 0)
    late_dots = jnp.concatenate([dots_all, jnp.zeros((pad_rows, HEADS), dots_all.dtype)], 0)
    late_owner = jnp.concatenate([documents, jnp.full((pad_rows,), -2, jnp.int32)], 0)

    def key_block(block_index):
        row_start = (block_index * BLK).astype(jnp.int32)
        key_rows = lax.dynamic_slice_in_dim(ordered_keys, row_start, BLK, 0).astype(jnp.float32)
        value_rows = lax.dynamic_slice_in_dim(ordered_values, row_start, BLK, 0).astype(jnp.float32)
        query_window = lax.dynamic_slice_in_dim(late_queries, row_start, window_rows, 0).astype(jnp.float32)
        output_window = lax.dynamic_slice_in_dim(late_outputs, row_start, window_rows, 0).astype(jnp.float32)
        total_window = lax.dynamic_slice_in_dim(late_totals, row_start, window_rows, 0)
        dot_window = lax.dynamic_slice_in_dim(late_dots, row_start, window_rows, 0)
        key_owner = lax.dynamic_slice_in_dim(documents, row_start, BLK, 0)
        query_owner = lax.dynamic_slice_in_dim(late_owner, row_start, window_rows, 0)
        key_place = row_start + block_offsets
        query_place = row_start + window_offsets
        allowed = (key_place[None, :] <= query_place[:, None]) & (query_place[:, None] < TOKENS) & (query_owner[:, None] == key_owner[None, :])
        scores = jnp.einsum('whd,bd->hwb', query_window, key_rows) * factor
        grad_prob = jnp.einsum('whd,bd->hwb', output_window, value_rows)
        probabilities = jnp.where(allowed[None], jnp.exp(scores - total_window.T[..., None]), 0.0)
        grad_scores = probabilities * (grad_prob - dot_window.T[..., None])
        value_grads = jnp.einsum('hwb,whd->bd', rounded(probabilities), output_window)
        key_grads = jnp.einsum('hwb,whd->bd', rounded(grad_scores), query_window) * factor
        return (key_grads.astype(jnp.bfloat16), value_grads.astype(jnp.bfloat16))
    key_blocks, value_blocks = lax.map(key_block, jnp.arange(BLOCKS, dtype=jnp.int32))
    grad_key_rows = key_blocks.reshape(TOKENS, D_HEAD)
    grad_value_rows = value_blocks.reshape(TOKENS, D_HEAD)
    return (to_stored(grad_query_rows, block_order), to_stored(grad_key_rows, block_order), to_stored(grad_value_rows, block_order))
```

```python
import math

import jax
import jax.numpy as jnp
import numpy as np
from jax import lax
from jax.sharding import PartitionSpec as P

REACH = 6

NEGATIVE = -1e30

AXES = ("outer", "inner")


def slot_tables(count):
    slots = 2 + 3 * REACH
    place = np.full((count, slots), -1, np.int64)
    for d in range(count):
        place[d, 0] = d
        place[d, 1] = 2 * count - 1 - d
        for k in range(1, REACH + 1):
            if d - k >= 0:
                place[d, 2 + k - 1] = d - k
            if d + k <= count - 1:
                place[d, 2 + REACH + 2 * (k - 1)] = d + k
                place[d, 3 + REACH + 2 * (k - 1)] = 2 * count - 1 - d - k
    window = np.zeros((count, 2, REACH + 1), np.int32)
    key_block = np.full((count, 2, REACH + 1), -1, np.int32)
    sources = np.full((count, slots, 2), 2 * (REACH + 1), np.int32)
    for d in range(count):
        filled = np.zeros(slots, np.int64)
        for q, query_block in enumerate((d, 2 * count - 1 - d)):
            for k in range(REACH + 1):
                target = query_block - (REACH - k)
                found = np.nonzero(place[d] == target)[0] if target >= 0 else []
                if len(found) == 0:
                    assert target < 0
                    continue
                m = int(found[0])
                window[d, q, k] = m
                key_block[d, q, k] = target
                sources[d, m, filled[m]] = q * (REACH + 1) + k
                filled[m] += 1
    return window, key_block, sources


def on_device(queries, key_states, value_states, grad_output, documents, block_order):
    count = lax.axis_size(AXES)
    device = lax.axis_index(AXES)
    length = key_states.shape[0] // 2
    head_size = key_states.shape[1]
    factor = 1.0 / math.sqrt(head_size)
    span = REACH + 1
    window_np, key_block_np, sources_np = slot_tables(count)

    first_slot = jnp.where(block_order[2 * device] < count, 0, 1).astype(jnp.int32)
    second_slot = 1 - first_slot

    def take_block(rows, slot):
        return lax.dynamic_slice_in_dim(rows, slot * length, length, 0)

    joined = jnp.concatenate([key_states, value_states], 1)
    low = take_block(joined, first_slot)
    high = take_block(joined, second_slot)
    both = jnp.concatenate([low, high], 0)

    received_low = []
    received_both = []
    for k in range(1, REACH + 1):
        up = [(s, s + k) for s in range(count - k)]
        down = [(s, s - k) for s in range(k, count)]
        received_low.append(lax.ppermute(low, AXES, up))
        received_both.append(lax.ppermute(both, AXES, down))
    held = [low, high] + received_low
    for pair in received_both:
        held += [pair[:length], pair[length:]]
    held = jnp.stack(held)

    window_idx = jnp.asarray(window_np)[device].reshape(-1)
    key_blocks = jnp.asarray(key_block_np)[device]
    windows = jnp.take(held, window_idx, axis=0).reshape(2, span * length, 2 * head_size)
    key_window = windows[..., :head_size]
    value_window = windows[..., head_size:]

    def split_heads(rows):
        return rows.reshape(rows.shape[0], rows.shape[1] // head_size, head_size)

    query_pair = jnp.stack(
        [split_heads(take_block(queries, first_slot)), split_heads(take_block(queries, second_slot))]
    )
    output_pair = jnp.stack(
        [
            split_heads(take_block(grad_output, first_slot)),
            split_heads(take_block(grad_output, second_slot)),
        ]
    )

    query_blocks = jnp.stack([device, 2 * count - 1 - device])
    offsets = jnp.arange(length, dtype=jnp.int32)
    query_place = query_blocks[:, None] * length + offsets[None, :]
    key_place = (key_blocks[:, :, None] * length + offsets[None, None, :]).reshape(2, span * length)
    query_owner = jnp.take(documents, query_place)
    key_owner = jnp.take(documents, jnp.maximum(key_place, 0))
    allowed = (
        (key_place[:, None, :] >= 0)
        & (key_place[:, None, :] <= query_place[:, :, None])
        & (key_owner[:, None, :] == query_owner[:, :, None])
    )[:, None]

    scores = (
        jnp.einsum("qbhd,qwd->qhbw", query_pair, key_window, preferred_element_type=jnp.float32)
        * factor
    )
    grad_prob = jnp.einsum(
        "qbhd,qwd->qhbw", output_pair, value_window, preferred_element_type=jnp.float32
    )
    masked = jnp.where(allowed, scores, NEGATIVE)
    top = masked.max(-1)
    weights = jnp.where(allowed, jnp.exp(scores - top[..., None]), 0.0)
    log_totals = top + jnp.log(weights.sum(-1))
    probabilities = jnp.where(allowed, jnp.exp(scores - log_totals[..., None]), 0.0)
    row_dots = (probabilities * grad_prob).sum(-1)
    grad_scores = probabilities * (grad_prob - row_dots[..., None])
    rounded_probs = probabilities.astype(jnp.bfloat16)
    rounded_grads = grad_scores.astype(jnp.bfloat16)

    grad_query = jnp.einsum(
        "qhbw,qwd->qbhd", rounded_grads, key_window, preferred_element_type=jnp.float32
    )
    grad_key = jnp.einsum(
        "qhbw,qbhd->qwd", rounded_grads, query_pair, preferred_element_type=jnp.float32
    )
    grad_value = jnp.einsum(
        "qhbw,qbhd->qwd", rounded_probs, output_pair, preferred_element_type=jnp.float32
    )
    parts = jnp.concatenate([grad_key, grad_value], -1).reshape(2 * span, length, 2 * head_size)
    parts = jnp.concatenate([parts, jnp.zeros((1,) + parts.shape[1:], parts.dtype)], 0)
    sources = jnp.asarray(sources_np)[device]
    summed = jnp.take(parts, sources[:, 0], axis=0) + jnp.take(parts, sources[:, 1], axis=0)

    grad_low = summed[0]
    grad_high = summed[1]
    for k in range(1, REACH + 1):
        up = [(s + k, s) for s in range(count - k)]
        down = [(s - k, s) for s in range(k, count)]
        grad_low = grad_low + lax.ppermute(summed[2 + k - 1], AXES, up)
        back = lax.ppermute(
            jnp.concatenate(
                [summed[2 + REACH + 2 * (k - 1)], summed[3 + REACH + 2 * (k - 1)]], 0
            ),
            AXES,
            down,
        )
        grad_low = grad_low + back[:length]
        grad_high = grad_high + back[length:]

    grad_query = (
        (grad_query * factor).astype(jnp.bfloat16).reshape(2, length, query_pair.shape[2] * head_size)
    )
    grad_kv = jnp.stack([grad_low, grad_high])
    grad_keys = (grad_kv[:, :, :head_size] * factor).astype(jnp.bfloat16)
    grad_values = grad_kv[:, :, head_size:].astype(jnp.bfloat16)

    def restore(paired):
        return jnp.concatenate([paired[first_slot], paired[second_slot]], 0)

    return (restore(grad_query), restore(grad_keys), restore(grad_values))


def solution(mesh):
    in_specs = (
        P(AXES, None),
        P(AXES, None),
        P(AXES, None),
        P(AXES, None),
        P(),
        P(),
    )
    out_specs = (
        P(AXES, None),
        P(AXES, None),
        P(AXES, None),
    )
    return jax.shard_map(
        on_device, mesh=mesh, in_specs=in_specs, out_specs=out_specs, check_vma=False
    )
```

```python
import math

import jax
import jax.numpy as jnp
import numpy as np
from jax import lax
from jax.sharding import PartitionSpec as P

REACH = 6

NEGATIVE = -1e30

AXES = ("outer", "inner")


def slot_tables(count):
    slots = 2 + 3 * REACH
    place = np.full((count, slots), -1, np.int64)
    for d in range(count):
        place[d, 0] = d
        place[d, 1] = 2 * count - 1 - d
        for k in range(1, REACH + 1):
            if d - k >= 0:
                place[d, 2 + k - 1] = d - k
            if d + k <= count - 1:
                place[d, 2 + REACH + 2 * (k - 1)] = d + k
                place[d, 3 + REACH + 2 * (k - 1)] = 2 * count - 1 - d - k
    window = np.zeros((count, 2, REACH + 1), np.int32)
    key_block = np.full((count, 2, REACH + 1), -1, np.int32)
    sources = np.full((count, slots, 2), 2 * (REACH + 1), np.int32)
    for d in range(count):
        filled = np.zeros(slots, np.int64)
        for q, query_block in enumerate((d, 2 * count - 1 - d)):
            for k in range(REACH + 1):
                target = query_block - (REACH - k)
                found = np.nonzero(place[d] == target)[0] if target >= 0 else []
                if len(found) == 0:
                    assert target < 0
                    continue
                m = int(found[0])
                window[d, q, k] = m
                key_block[d, q, k] = target
                sources[d, m, filled[m]] = q * (REACH + 1) + k
                filled[m] += 1
    return window, key_block, sources


def on_device(queries, key_states, value_states, grad_output, documents, block_order):
    count = lax.axis_size(AXES)
    device = lax.axis_index(AXES)
    length = key_states.shape[0] // 2
    head_size = key_states.shape[1]
    factor = 1.0 / math.sqrt(head_size)
    span = REACH + 1
    window_np, key_block_np, sources_np = slot_tables(count)

    first_slot = jnp.where(block_order[2 * device] < count, 0, 1).astype(jnp.int32)
    second_slot = 1 - first_slot

    def take_block(rows, slot):
        return lax.dynamic_slice_in_dim(rows, slot * length, length, 0)

    joined = jnp.concatenate([key_states, value_states], 1)
    low = take_block(joined, first_slot)
    high = take_block(joined, second_slot)
    both = jnp.concatenate([low, high], 0)

    received_low = []
    received_both = []
    for k in range(1, REACH + 1):
        up = [(s, s + k) for s in range(count - k)]
        down = [(s, s - k) for s in range(k, count)]
        received_low.append(lax.ppermute(low, AXES, up))
        received_both.append(lax.ppermute(both, AXES, down))
    held = [low, high] + received_low
    for pair in received_both:
        held += [pair[:length], pair[length:]]
    held = jnp.stack(held)

    window_idx = jnp.asarray(window_np)[device].reshape(-1)
    key_blocks = jnp.asarray(key_block_np)[device]
    windows = jnp.stack(
        [lax.dynamic_index_in_dim(held, window_idx[i], 0, keepdims=False) for i in range(2 * span)]
    ).reshape(2, span * length, 2 * head_size)
    key_window = windows[..., :head_size]
    value_window = windows[..., head_size:]

    def split_heads(rows):
        return rows.reshape(rows.shape[0], rows.shape[1] // head_size, head_size)

    query_pair = jnp.stack(
        [split_heads(take_block(queries, first_slot)), split_heads(take_block(queries, second_slot))]
    )
    output_pair = jnp.stack(
        [
            split_heads(take_block(grad_output, first_slot)),
            split_heads(take_block(grad_output, second_slot)),
        ]
    )

    query_blocks = jnp.stack([device, 2 * count - 1 - device])
    offsets = jnp.arange(length, dtype=jnp.int32)
    query_place = query_blocks[:, None] * length + offsets[None, :]
    key_place = (key_blocks[:, :, None] * length + offsets[None, None, :]).reshape(2, span * length)
    query_owner = jnp.stack(
        [lax.dynamic_slice_in_dim(documents, query_blocks[q] * length, length) for q in range(2)]
    )
    safe_blocks = jnp.maximum(key_blocks, 0)
    key_owner = jnp.stack(
        [
            jnp.concatenate(
                [
                    lax.dynamic_slice_in_dim(documents, safe_blocks[q, k] * length, length)
                    for k in range(span)
                ]
            )
            for q in range(2)
        ]
    )
    allowed = (
        (key_place[:, None, :] >= 0)
        & (key_place[:, None, :] <= query_place[:, :, None])
        & (key_owner[:, None, :] == query_owner[:, :, None])
    )[:, None]

    scores = (
        jnp.einsum("qbhd,qwd->qhbw", query_pair, key_window, preferred_element_type=jnp.float32)
        * factor
    )
    grad_prob = jnp.einsum(
        "qbhd,qwd->qhbw", output_pair, value_window, preferred_element_type=jnp.float32
    )
    masked = jnp.where(allowed, scores, NEGATIVE)
    top = masked.max(-1)
    weights = jnp.where(allowed, jnp.exp(scores - top[..., None]), 0.0)
    log_totals = top + jnp.log(weights.sum(-1))
    probabilities = jnp.where(allowed, jnp.exp(scores - log_totals[..., None]), 0.0)
    row_dots = (probabilities * grad_prob).sum(-1)
    grad_scores = probabilities * (grad_prob - row_dots[..., None])
    rounded_probs = probabilities.astype(jnp.bfloat16)
    rounded_grads = grad_scores.astype(jnp.bfloat16)

    grad_query = jnp.einsum(
        "qhbw,qwd->qbhd", rounded_grads, key_window, preferred_element_type=jnp.float32
    )
    grad_key = jnp.einsum(
        "qhbw,qbhd->qwd", rounded_grads, query_pair, preferred_element_type=jnp.float32
    )
    grad_value = jnp.einsum(
        "qhbw,qbhd->qwd", rounded_probs, output_pair, preferred_element_type=jnp.float32
    )
    parts = jnp.concatenate([grad_key, grad_value], -1).reshape(2 * span, length, 2 * head_size)
    parts = jnp.concatenate([parts, jnp.zeros((1,) + parts.shape[1:], parts.dtype)], 0)
    sources = jnp.asarray(sources_np)[device]
    summed = [
        lax.dynamic_index_in_dim(parts, sources[m, 0], 0, keepdims=False)
        + lax.dynamic_index_in_dim(parts, sources[m, 1], 0, keepdims=False)
        for m in range(sources_np.shape[1])
    ]

    grad_low = summed[0]
    grad_high = summed[1]
    for k in range(1, REACH + 1):
        up = [(s + k, s) for s in range(count - k)]
        down = [(s - k, s) for s in range(k, count)]
        grad_low = grad_low + lax.ppermute(summed[2 + k - 1], AXES, up)
        back = lax.ppermute(
            jnp.concatenate(
                [summed[2 + REACH + 2 * (k - 1)], summed[3 + REACH + 2 * (k - 1)]], 0
            ),
            AXES,
            down,
        )
        grad_low = grad_low + back[:length]
        grad_high = grad_high + back[length:]

    grad_query = (
        (grad_query * factor).astype(jnp.bfloat16).reshape(2, length, query_pair.shape[2] * head_size)
    )
    grad_kv = jnp.stack([grad_low, grad_high])
    grad_keys = (grad_kv[:, :, :head_size] * factor).astype(jnp.bfloat16)
    grad_values = grad_kv[:, :, head_size:].astype(jnp.bfloat16)

    def restore(paired):
        return jnp.concatenate([paired[first_slot], paired[second_slot]], 0)

    return (restore(grad_query), restore(grad_keys), restore(grad_values))


def solution(mesh):
    in_specs = (
        P(AXES, None),
        P(AXES, None),
        P(AXES, None),
        P(AXES, None),
        P(),
        P(),
    )
    out_specs = (
        P(AXES, None),
        P(AXES, None),
        P(AXES, None),
    )
    return jax.shard_map(
        on_device, mesh=mesh, in_specs=in_specs, out_specs=out_specs, check_vma=False
    )
```

```python
import math

import jax
import jax.numpy as jnp
from jax import lax
from jax.sharding import PartitionSpec as P

REACH = 6

NEGATIVE = -1e30

AXES = ("outer", "inner")


def fold_source(r, j):
    if j <= r:
        return ("high", j)
    gap = 2 * r + 1 - j
    if gap > 0:
        return ("above", gap)
    if gap == 0:
        return ("own", 0)
    return ("below", -gap)


def on_device(queries, key_states, value_states, grad_output, documents, block_order):
    count = lax.axis_size(AXES)
    device = lax.axis_index(AXES)
    length = key_states.shape[0] // 2
    head_size = key_states.shape[1]
    factor = 1.0 / math.sqrt(head_size)
    span = REACH + 1

    first_slot = jnp.where(block_order[2 * device] < count, 0, 1).astype(jnp.int32)
    second_slot = 1 - first_slot

    def take_block(rows, slot):
        return lax.dynamic_slice_in_dim(rows, slot * length, length, 0)

    joined = jnp.concatenate([key_states, value_states], 1)
    low = take_block(joined, first_slot)
    high = take_block(joined, second_slot)
    both = jnp.concatenate([low, high], 0)

    below = {}
    above_low = {}
    above_high = {}
    for k in range(1, REACH + 1):
        up = [(s, s + k) for s in range(count - k)]
        down = [(s, s - k) for s in range(k, count)]
        below[k] = lax.ppermute(low, AXES, up)
        pair = lax.ppermute(both, AXES, down)
        above_low[k] = pair[:length]
        above_high[k] = pair[length:]

    low_window = jnp.concatenate([below[j] for j in range(REACH, 0, -1)] + [low], 0)

    def high_window_for(r):
        def build(operands):
            below_, above_low_, above_high_, low_, high_ = operands
            named = {"high": above_high_, "above": above_low_, "below": below_}
            pieces = []
            for j in range(REACH, 0, -1):
                kind, at = fold_source(r, j)
                pieces.append(low_ if kind == "own" else named[kind][at - 1])
            return jnp.concatenate(pieces + [high_], 0)

        return build

    fold_index = jnp.clip(count - 1 - device, 0, REACH)
    operands = (
        [below[j] for j in range(1, REACH + 1)],
        [above_low[j] for j in range(1, REACH + 1)],
        [above_high[j] for j in range(1, REACH + 1)],
        low,
        high,
    )
    high_window = lax.switch(fold_index, [high_window_for(r) for r in range(REACH + 1)], operands)
    windows = jnp.stack([low_window, high_window])
    key_window = windows[..., :head_size]
    value_window = windows[..., head_size:]

    def split_heads(rows):
        return rows.reshape(rows.shape[0], rows.shape[1] // head_size, head_size)

    query_pair = jnp.stack(
        [split_heads(take_block(queries, first_slot)), split_heads(take_block(queries, second_slot))]
    )
    output_pair = jnp.stack(
        [
            split_heads(take_block(grad_output, first_slot)),
            split_heads(take_block(grad_output, second_slot)),
        ]
    )

    pad = REACH * length
    padded_documents = jnp.concatenate([jnp.full((pad,), -1, documents.dtype), documents])
    query_blocks = (device, 2 * count - 1 - device)
    offsets = jnp.arange(length, dtype=jnp.int32)
    window_offsets = jnp.arange(span * length, dtype=jnp.int32)
    query_place = jnp.stack([b * length + offsets for b in query_blocks])
    key_place = jnp.stack([b * length - pad + window_offsets for b in query_blocks])
    query_owner = jnp.stack(
        [lax.dynamic_slice_in_dim(documents, b * length, length) for b in query_blocks]
    )
    key_owner = jnp.stack(
        [lax.dynamic_slice_in_dim(padded_documents, b * length, span * length) for b in query_blocks]
    )
    allowed = (
        (key_place[:, None, :] >= 0)
        & (key_place[:, None, :] <= query_place[:, :, None])
        & (key_owner[:, None, :] == query_owner[:, :, None])
    )[:, None]

    scores = (
        jnp.einsum("qbhd,qwd->qhbw", query_pair, key_window, preferred_element_type=jnp.float32)
        * factor
    )
    grad_prob = jnp.einsum(
        "qbhd,qwd->qhbw", output_pair, value_window, preferred_element_type=jnp.float32
    )
    masked = jnp.where(allowed, scores, NEGATIVE)
    top = masked.max(-1)
    weights = jnp.where(allowed, jnp.exp(scores - top[..., None]), 0.0)
    log_totals = top + jnp.log(weights.sum(-1))
    probabilities = jnp.where(allowed, jnp.exp(scores - log_totals[..., None]), 0.0)
    row_dots = (probabilities * grad_prob).sum(-1)
    grad_scores = probabilities * (grad_prob - row_dots[..., None])
    rounded_probs = probabilities.astype(jnp.bfloat16)
    rounded_grads = grad_scores.astype(jnp.bfloat16)

    grad_query = jnp.einsum(
        "qhbw,qwd->qbhd", rounded_grads, key_window, preferred_element_type=jnp.float32
    )
    grad_key = jnp.einsum(
        "qhbw,qbhd->qwd", rounded_grads, query_pair, preferred_element_type=jnp.float32
    )
    grad_value = jnp.einsum(
        "qhbw,qbhd->qwd", rounded_probs, output_pair, preferred_element_type=jnp.float32
    )
    parts = jnp.concatenate([grad_key, grad_value], -1).reshape(2, span, length, 2 * head_size)
    low_parts = parts[0]
    high_parts = parts[1]

    def high_parts_for(r):
        def route(blocks):
            zero = jnp.zeros_like(blocks[0])
            slots = {
                "high": [zero] * REACH,
                "above": [zero] * REACH,
                "below": [zero] * REACH,
                "own": [zero],
            }
            for j in range(REACH, 0, -1):
                kind, at = fold_source(r, j)
                slots[kind][max(at, 1) - 1] = blocks[REACH - j]
            return (
                jnp.stack(slots["high"]),
                jnp.stack(slots["above"]),
                jnp.stack(slots["below"]),
                slots["own"][0],
            )

        return route

    to_high, to_above_low, to_below, to_own_low = lax.switch(
        fold_index, [high_parts_for(r) for r in range(REACH + 1)], high_parts
    )

    grad_low = low_parts[REACH] + to_own_low
    grad_high = high_parts[REACH]
    for k in range(1, REACH + 1):
        up = [(s + k, s) for s in range(count - k)]
        down = [(s - k, s) for s in range(k, count)]
        grad_low = grad_low + lax.ppermute(low_parts[REACH - k] + to_below[k - 1], AXES, up)
        back = lax.ppermute(
            jnp.concatenate([to_above_low[k - 1], to_high[k - 1]], 0), AXES, down
        )
        grad_low = grad_low + back[:length]
        grad_high = grad_high + back[length:]

    grad_query = (
        (grad_query * factor).astype(jnp.bfloat16).reshape(2, length, query_pair.shape[2] * head_size)
    )
    grad_kv = jnp.stack([grad_low, grad_high])
    grad_keys = (grad_kv[:, :, :head_size] * factor).astype(jnp.bfloat16)
    grad_values = grad_kv[:, :, head_size:].astype(jnp.bfloat16)

    def restore(paired):
        return jnp.concatenate([paired[first_slot], paired[second_slot]], 0)

    return (restore(grad_query), restore(grad_keys), restore(grad_values))


def solution(mesh):
    in_specs = (
        P(AXES, None),
        P(AXES, None),
        P(AXES, None),
        P(AXES, None),
        P(),
        P(),
    )
    out_specs = (
        P(AXES, None),
        P(AXES, None),
        P(AXES, None),
    )
    return jax.shard_map(
        on_device, mesh=mesh, in_specs=in_specs, out_specs=out_specs, check_vma=False
    )
```

```python
import math

import jax
import jax.numpy as jnp
import numpy as np
from jax import lax
from jax.sharding import PartitionSpec as P

REACH = 6

NEGATIVE = -1e30

AXES = ("outer", "inner")

CHIP_REACH = REACH // 2


def slot_places(count):
    slots = 4 + 2 * CHIP_REACH + 4 * CHIP_REACH
    place = np.full((count, slots), -1, np.int64)

    def chip_blocks(chip):
        if chip < 0 or chip >= count // 2:
            return [-1, -1, -1, -1]
        return [2 * chip, 2 * chip + 1, 2 * count - 1 - 2 * chip, 2 * count - 2 - 2 * chip]

    for d in range(count):
        c = d // 2
        row = chip_blocks(c)
        for j in range(1, CHIP_REACH + 1):
            row += chip_blocks(c - j)[:2]
        for j in range(1, CHIP_REACH + 1):
            row += chip_blocks(c + j)
        place[d] = row
    return place


def routing_tables(count):
    place = slot_places(count)
    span = REACH + 1
    pick = np.zeros((count, 2 * span, place.shape[1]), np.float32)
    for d in range(count):
        for q, query_block in enumerate((d, 2 * count - 1 - d)):
            for k in range(span):
                target = query_block - REACH + k
                if target < 0:
                    continue
                found = np.nonzero(place[d] == target)[0]
                assert len(found) == 1
                pick[d, q * span + k, found[0]] = 1.0
    return pick


def on_device(queries, key_states, value_states, grad_output, documents, block_order):
    count = lax.axis_size(AXES)
    device = lax.axis_index(AXES)
    length = key_states.shape[0] // 2
    head_size = key_states.shape[1]
    factor = 1.0 / math.sqrt(head_size)
    span = REACH + 1
    pick = jnp.asarray(routing_tables(count))[device]
    odd = (device % 2) == 1

    first_slot = jnp.where(block_order[2 * device] < count, 0, 1).astype(jnp.int32)
    second_slot = 1 - first_slot

    def take_block(rows, slot):
        return lax.dynamic_slice_in_dim(rows, slot * length, length, 0)

    joined = jnp.concatenate([key_states, value_states], 1)
    own = jnp.stack([take_block(joined, first_slot), take_block(joined, second_slot)])
    mate_pairs = [(s, s ^ 1) for s in range(count)]
    mate = lax.ppermute(own, AXES, mate_pairs)
    even_part = jnp.where(odd, mate, own)
    odd_part = jnp.where(odd, own, mate)
    chip = jnp.stack([even_part[0], odd_part[0], even_part[1], odd_part[1]])

    held = [chip]
    for j in range(1, CHIP_REACH + 1):
        up = [(s, s + 2 * j) for s in range(count - 2 * j)]
        held.append(lax.ppermute(chip[:2], AXES, up))
    for j in range(1, CHIP_REACH + 1):
        down = [(s, s - 2 * j) for s in range(2 * j, count)]
        held.append(lax.ppermute(chip, AXES, down))
    held = jnp.concatenate(held, 0)

    windows = jnp.einsum(
        "ws,src->wrc", pick.astype(jnp.bfloat16), held, preferred_element_type=jnp.float32
    ).astype(jnp.bfloat16)
    windows = windows.reshape(2, span * length, 2 * head_size)
    key_window = windows[..., :head_size]
    value_window = windows[..., head_size:]

    def split_heads(rows):
        return rows.reshape(rows.shape[0], rows.shape[1] // head_size, head_size)

    query_pair = jnp.stack(
        [split_heads(take_block(queries, first_slot)), split_heads(take_block(queries, second_slot))]
    )
    output_pair = jnp.stack(
        [
            split_heads(take_block(grad_output, first_slot)),
            split_heads(take_block(grad_output, second_slot)),
        ]
    )

    pad = REACH * length
    padded_documents = jnp.concatenate([jnp.full((pad,), -1, documents.dtype), documents])
    query_blocks = (device, 2 * count - 1 - device)
    offsets = jnp.arange(length, dtype=jnp.int32)
    window_offsets = jnp.arange(span * length, dtype=jnp.int32)
    query_place = jnp.stack([b * length + offsets for b in query_blocks])
    key_place = jnp.stack([b * length - pad + window_offsets for b in query_blocks])
    query_owner = jnp.stack(
        [lax.dynamic_slice_in_dim(documents, b * length, length) for b in query_blocks]
    )
    key_owner = jnp.stack(
        [lax.dynamic_slice_in_dim(padded_documents, b * length, span * length) for b in query_blocks]
    )
    allowed = (
        (key_place[:, None, :] >= 0)
        & (key_place[:, None, :] <= query_place[:, :, None])
        & (key_owner[:, None, :] == query_owner[:, :, None])
    )[:, None]

    scores = (
        jnp.einsum("qbhd,qwd->qhbw", query_pair, key_window, preferred_element_type=jnp.float32)
        * factor
    )
    grad_prob = jnp.einsum(
        "qbhd,qwd->qhbw", output_pair, value_window, preferred_element_type=jnp.float32
    )
    masked = jnp.where(allowed, scores, NEGATIVE)
    top = masked.max(-1)
    weights = jnp.where(allowed, jnp.exp(scores - top[..., None]), 0.0)
    log_totals = top + jnp.log(weights.sum(-1))
    probabilities = jnp.where(allowed, jnp.exp(scores - log_totals[..., None]), 0.0)
    row_dots = (probabilities * grad_prob).sum(-1)
    grad_scores = probabilities * (grad_prob - row_dots[..., None])
    rounded_probs = probabilities.astype(jnp.bfloat16)
    rounded_grads = grad_scores.astype(jnp.bfloat16)

    grad_query = jnp.einsum(
        "qhbw,qwd->qbhd", rounded_grads, key_window, preferred_element_type=jnp.float32
    )
    grad_key = jnp.einsum(
        "qhbw,qbhd->qwd", rounded_grads, query_pair, preferred_element_type=jnp.float32
    )
    grad_value = jnp.einsum(
        "qhbw,qbhd->qwd", rounded_probs, output_pair, preferred_element_type=jnp.float32
    )
    parts = jnp.concatenate([grad_key, grad_value], -1).reshape(2 * span, length, 2 * head_size)
    gathered = jnp.einsum(
        "ws,wrc->src", pick, parts, precision=lax.Precision.HIGHEST,
        preferred_element_type=jnp.float32,
    )

    chip_total = gathered[:4]
    at = 4
    for j in range(1, CHIP_REACH + 1):
        up = [(s + 2 * j, s) for s in range(count - 2 * j)]
        back = lax.ppermute(gathered[at : at + 2], AXES, up)
        chip_total = chip_total + jnp.concatenate([back, jnp.zeros_like(back)], 0)
        at += 2
    for j in range(1, CHIP_REACH + 1):
        down = [(s - 2 * j, s) for s in range(2 * j, count)]
        chip_total = chip_total + lax.ppermute(gathered[at : at + 4], AXES, down)
        at += 4
    even_total = jnp.stack([chip_total[0], chip_total[2]])
    odd_total = jnp.stack([chip_total[1], chip_total[3]])
    mine = jnp.where(odd, odd_total, even_total)
    theirs = jnp.where(odd, even_total, odd_total)
    grad_kv = mine + lax.ppermute(theirs, AXES, mate_pairs)

    grad_query = (
        (grad_query * factor).astype(jnp.bfloat16).reshape(2, length, query_pair.shape[2] * head_size)
    )
    grad_keys = (grad_kv[:, :, :head_size] * factor).astype(jnp.bfloat16)
    grad_values = grad_kv[:, :, head_size:].astype(jnp.bfloat16)

    def restore(paired):
        return jnp.concatenate([paired[first_slot], paired[second_slot]], 0)

    return (restore(grad_query), restore(grad_keys), restore(grad_values))


def solution(mesh):
    in_specs = (
        P(AXES, None),
        P(AXES, None),
        P(AXES, None),
        P(AXES, None),
        P(),
        P(),
    )
    out_specs = (
        P(AXES, None),
        P(AXES, None),
        P(AXES, None),
    )
    return jax.shard_map(
        on_device, mesh=mesh, in_specs=in_specs, out_specs=out_specs, check_vma=False
    )
```

```python
import math

import jax
import jax.numpy as jnp
from jax import lax
from jax.sharding import PartitionSpec as P

REACH = 6

NEGATIVE = -1e30

AXES = ("outer", "inner")


def fold_source(r, j):
    if j <= r:
        return ("high", j)
    gap = 2 * r + 1 - j
    if gap > 0:
        return ("above", gap)
    if gap == 0:
        return ("own", 0)
    return ("below", -gap)


def on_device(queries, key_states, value_states, grad_output, documents, block_order):
    count = lax.axis_size(AXES)
    device = lax.axis_index(AXES)
    length = key_states.shape[0] // 2
    head_size = key_states.shape[1]
    factor = 1.0 / math.sqrt(head_size)
    span = REACH + 1

    first_slot = jnp.where(block_order[2 * device] < count, 0, 1).astype(jnp.int32)
    second_slot = 1 - first_slot

    def take_block(rows, slot):
        return lax.dynamic_slice_in_dim(rows, slot * length, length, 0)

    joined = jnp.concatenate([key_states, value_states], 1)
    low = take_block(joined, first_slot)
    high = take_block(joined, second_slot)
    both = jnp.concatenate([low, high], 0)

    below = {}
    above_low = {}
    above_high = {}
    for k in range(1, REACH + 1):
        up = [(s, s + k) for s in range(count - k)]
        down = [(s, s - k) for s in range(k, count)]
        below[k] = lax.ppermute(low, AXES, up)
        pair = lax.ppermute(both, AXES, down)
        above_low[k] = pair[:length]
        above_high[k] = pair[length:]

    low_window = jnp.concatenate([below[j] for j in range(REACH, 0, -1)] + [low], 0)

    fold_index = jnp.clip(count - 1 - device, 0, REACH)
    named = {"high": above_high, "above": above_low, "below": below}

    def source_block(kind, at):
        return low if kind == "own" else named[kind][at]

    pieces = []
    for j in range(REACH, 0, -1):
        block = above_high[j]
        for r in range(j - 1, -1, -1):
            block = jnp.where(fold_index == r, source_block(*fold_source(r, j)), block)
        pieces.append(block)
    high_window = jnp.concatenate(pieces + [high], 0)
    windows = jnp.stack([low_window, high_window])
    key_window = windows[..., :head_size]
    value_window = windows[..., head_size:]

    def split_heads(rows):
        return rows.reshape(rows.shape[0], rows.shape[1] // head_size, head_size)

    query_pair = jnp.stack(
        [split_heads(take_block(queries, first_slot)), split_heads(take_block(queries, second_slot))]
    )
    output_pair = jnp.stack(
        [
            split_heads(take_block(grad_output, first_slot)),
            split_heads(take_block(grad_output, second_slot)),
        ]
    )

    pad = REACH * length
    padded_documents = jnp.concatenate([jnp.full((pad,), -1, documents.dtype), documents])
    query_blocks = (device, 2 * count - 1 - device)
    offsets = jnp.arange(length, dtype=jnp.int32)
    window_offsets = jnp.arange(span * length, dtype=jnp.int32)
    query_place = jnp.stack([b * length + offsets for b in query_blocks])
    key_place = jnp.stack([b * length - pad + window_offsets for b in query_blocks])
    query_owner = jnp.stack(
        [lax.dynamic_slice_in_dim(documents, b * length, length) for b in query_blocks]
    )
    key_owner = jnp.stack(
        [lax.dynamic_slice_in_dim(padded_documents, b * length, span * length) for b in query_blocks]
    )
    allowed = (
        (key_place[:, None, :] >= 0)
        & (key_place[:, None, :] <= query_place[:, :, None])
        & (key_owner[:, None, :] == query_owner[:, :, None])
    )[:, None]

    scores = (
        jnp.einsum("qbhd,qwd->qhbw", query_pair, key_window, preferred_element_type=jnp.float32)
        * factor
    )
    grad_prob = jnp.einsum(
        "qbhd,qwd->qhbw", output_pair, value_window, preferred_element_type=jnp.float32
    )
    masked = jnp.where(allowed, scores, NEGATIVE)
    top = masked.max(-1)
    weights = jnp.where(allowed, jnp.exp(scores - top[..., None]), 0.0)
    log_totals = top + jnp.log(weights.sum(-1))
    probabilities = jnp.where(allowed, jnp.exp(scores - log_totals[..., None]), 0.0)
    row_dots = (probabilities * grad_prob).sum(-1)
    grad_scores = probabilities * (grad_prob - row_dots[..., None])
    rounded_probs = probabilities.astype(jnp.bfloat16)
    rounded_grads = grad_scores.astype(jnp.bfloat16)

    grad_query = jnp.einsum(
        "qhbw,qwd->qbhd", rounded_grads, key_window, preferred_element_type=jnp.float32
    )
    grad_key = jnp.einsum(
        "qhbw,qbhd->qwd", rounded_grads, query_pair, preferred_element_type=jnp.float32
    )
    grad_value = jnp.einsum(
        "qhbw,qbhd->qwd", rounded_probs, output_pair, preferred_element_type=jnp.float32
    )
    parts = jnp.concatenate([grad_key, grad_value], -1).reshape(2, span, length, 2 * head_size)
    low_parts = parts[0]
    high_parts = parts[1]

    zero = jnp.zeros_like(high_parts[0])
    routed = {}
    for r in range(REACH):
        for j in range(r + 1, REACH + 1):
            routed.setdefault(fold_source(r, j), []).append((r, j))

    def routed_to(kind, at):
        block = zero
        for r, j in routed.get((kind, at), []):
            block = jnp.where(fold_index == r, high_parts[REACH - j], block)
        return block

    to_high = [jnp.where(fold_index >= j, high_parts[REACH - j], zero) for j in range(1, REACH + 1)]
    to_above_low = [routed_to("above", m) for m in range(1, REACH + 1)]
    to_below = [routed_to("below", m) for m in range(1, REACH + 1)]
    to_own_low = routed_to("own", 0)

    grad_low = low_parts[REACH] + to_own_low
    grad_high = high_parts[REACH]
    for k in range(1, REACH + 1):
        up = [(s + k, s) for s in range(count - k)]
        down = [(s - k, s) for s in range(k, count)]
        grad_low = grad_low + lax.ppermute(low_parts[REACH - k] + to_below[k - 1], AXES, up)
        back = lax.ppermute(
            jnp.concatenate([to_above_low[k - 1], to_high[k - 1]], 0), AXES, down
        )
        grad_low = grad_low + back[:length]
        grad_high = grad_high + back[length:]

    grad_query = (
        (grad_query * factor).astype(jnp.bfloat16).reshape(2, length, query_pair.shape[2] * head_size)
    )
    grad_kv = jnp.stack([grad_low, grad_high])
    grad_keys = (grad_kv[:, :, :head_size] * factor).astype(jnp.bfloat16)
    grad_values = grad_kv[:, :, head_size:].astype(jnp.bfloat16)

    def restore(paired):
        return jnp.concatenate([paired[first_slot], paired[second_slot]], 0)

    return (restore(grad_query), restore(grad_keys), restore(grad_values))


def solution(mesh):
    in_specs = (
        P(AXES, None),
        P(AXES, None),
        P(AXES, None),
        P(AXES, None),
        P(),
        P(),
    )
    out_specs = (
        P(AXES, None),
        P(AXES, None),
        P(AXES, None),
    )
    return jax.shard_map(
        on_device, mesh=mesh, in_specs=in_specs, out_specs=out_specs, check_vma=False
    )
```

```python
import math

import jax
import jax.numpy as jnp
from jax import lax
from jax.sharding import PartitionSpec as P

REACH = 6

NEGATIVE = -1e30

AXES = ("outer", "inner")


def fold_source(r, j):
    if j <= r:
        return ("high", j)
    gap = 2 * r + 1 - j
    if gap > 0:
        return ("above", gap)
    if gap == 0:
        return ("own", 0)
    return ("below", -gap)


def on_device(queries, key_states, value_states, grad_output, documents, block_order):
    count = lax.axis_size(AXES)
    device = lax.axis_index(AXES)
    length = key_states.shape[0] // 2
    head_size = key_states.shape[1]
    factor = 1.0 / math.sqrt(head_size)
    span = REACH + 1

    first_slot = jnp.where(block_order[2 * device] < count, 0, 1).astype(jnp.int32)
    second_slot = 1 - first_slot

    def take_block(rows, slot):
        return lax.dynamic_slice_in_dim(rows, slot * length, length, 0)

    joined = jnp.concatenate([key_states, value_states], 1)
    low = take_block(joined, first_slot)
    high = take_block(joined, second_slot)
    odd = (device % 2) == 1
    own = jnp.stack([low, high])
    mate = lax.ppermute(own, AXES, [(s, s ^ 1) for s in range(count)])
    even_part = jnp.where(odd, mate, own)
    odd_part = jnp.where(odd, own, mate)
    chip = jnp.stack([even_part[0], odd_part[0], even_part[1], odd_part[1]])
    lows = {0: chip[0], 1: chip[1]}
    highs = {0: chip[2], 1: chip[3]}
    for j in range(1, REACH // 2 + 1):
        up = [(s, s + 2 * j) for s in range(count - 2 * j)]
        down = [(s, s - 2 * j) for s in range(2 * j, count)]
        below_chip = lax.ppermute(chip[:2], AXES, up)
        above_chip = lax.ppermute(chip, AXES, down)
        lows[-2 * j], lows[1 - 2 * j] = below_chip[0], below_chip[1]
        lows[2 * j], lows[2 * j + 1] = above_chip[0], above_chip[1]
        highs[2 * j], highs[2 * j + 1] = above_chip[2], above_chip[3]

    def by_parity(table, t):
        return jnp.where(odd, table[t + 1], table[t])

    low_window = jnp.concatenate([by_parity(lows, t) for t in range(-REACH, 1)], 0)

    fold_index = jnp.clip(count - 1 - device, 0, REACH)

    def fold_block(r, j):
        parity = (count - 1 - r) % 2
        kind, at = fold_source(r, j)
        return lows[parity + {"above": at, "own": 0, "below": -at}[kind]]

    pieces = []
    for j in range(REACH, 0, -1):
        block = by_parity(highs, j)
        for r in range(j - 1, -1, -1):
            block = jnp.where(fold_index == r, fold_block(r, j), block)
        pieces.append(block)
    high_window = jnp.concatenate(pieces + [by_parity(highs, 0)], 0)
    windows = jnp.stack([low_window, high_window])
    key_window = windows[..., :head_size]
    value_window = windows[..., head_size:]

    def split_heads(rows):
        return rows.reshape(rows.shape[0], rows.shape[1] // head_size, head_size)

    query_pair = jnp.stack(
        [split_heads(take_block(queries, first_slot)), split_heads(take_block(queries, second_slot))]
    )
    output_pair = jnp.stack(
        [
            split_heads(take_block(grad_output, first_slot)),
            split_heads(take_block(grad_output, second_slot)),
        ]
    )

    pad = REACH * length
    padded_documents = jnp.concatenate([jnp.full((pad,), -1, documents.dtype), documents])
    query_blocks = (device, 2 * count - 1 - device)
    offsets = jnp.arange(length, dtype=jnp.int32)
    window_offsets = jnp.arange(span * length, dtype=jnp.int32)
    query_place = jnp.stack([b * length + offsets for b in query_blocks])
    key_place = jnp.stack([b * length - pad + window_offsets for b in query_blocks])
    query_owner = jnp.stack(
        [lax.dynamic_slice_in_dim(documents, b * length, length) for b in query_blocks]
    )
    key_owner = jnp.stack(
        [lax.dynamic_slice_in_dim(padded_documents, b * length, span * length) for b in query_blocks]
    )
    allowed = (
        (key_place[:, None, :] >= 0)
        & (key_place[:, None, :] <= query_place[:, :, None])
        & (key_owner[:, None, :] == query_owner[:, :, None])
    )[:, None]

    scores = (
        jnp.einsum("qbhd,qwd->qhbw", query_pair, key_window, preferred_element_type=jnp.float32)
        * factor
    )
    grad_prob = jnp.einsum(
        "qbhd,qwd->qhbw", output_pair, value_window, preferred_element_type=jnp.float32
    )
    masked = jnp.where(allowed, scores, NEGATIVE)
    top = masked.max(-1)
    weights = jnp.where(allowed, jnp.exp(scores - top[..., None]), 0.0)
    log_totals = top + jnp.log(weights.sum(-1))
    probabilities = jnp.where(allowed, jnp.exp(scores - log_totals[..., None]), 0.0)
    row_dots = (probabilities * grad_prob).sum(-1)
    grad_scores = probabilities * (grad_prob - row_dots[..., None])
    rounded_probs = probabilities.astype(jnp.bfloat16)
    rounded_grads = grad_scores.astype(jnp.bfloat16)

    grad_query = jnp.einsum(
        "qhbw,qwd->qbhd", rounded_grads, key_window, preferred_element_type=jnp.float32
    )
    grad_key = jnp.einsum(
        "qhbw,qbhd->qwd", rounded_grads, query_pair, preferred_element_type=jnp.float32
    )
    grad_value = jnp.einsum(
        "qhbw,qbhd->qwd", rounded_probs, output_pair, preferred_element_type=jnp.float32
    )
    parts = jnp.concatenate([grad_key, grad_value], -1).reshape(2, span, length, 2 * head_size)
    low_parts = parts[0]
    high_parts = parts[1]

    zero = jnp.zeros_like(high_parts[0])
    routed = {}
    for r in range(REACH):
        for j in range(r + 1, REACH + 1):
            routed.setdefault(fold_source(r, j), []).append((r, j))

    def routed_to(kind, at):
        block = zero
        for r, j in routed.get((kind, at), []):
            block = jnp.where(fold_index == r, high_parts[REACH - j], block)
        return block

    to_high = [jnp.where(fold_index >= j, high_parts[REACH - j], zero) for j in range(1, REACH + 1)]
    to_above_low = [routed_to("above", m) for m in range(1, REACH + 1)]
    to_below = [routed_to("below", m) for m in range(1, REACH + 1)]
    to_own_low = routed_to("own", 0)

    grad_low = low_parts[REACH] + to_own_low
    grad_high = high_parts[REACH]
    for k in range(1, REACH + 1):
        up = [(s + k, s) for s in range(count - k)]
        down = [(s - k, s) for s in range(k, count)]
        grad_low = grad_low + lax.ppermute(low_parts[REACH - k] + to_below[k - 1], AXES, up)
        back = lax.ppermute(
            jnp.concatenate([to_above_low[k - 1], to_high[k - 1]], 0), AXES, down
        )
        grad_low = grad_low + back[:length]
        grad_high = grad_high + back[length:]

    grad_query = (
        (grad_query * factor).astype(jnp.bfloat16).reshape(2, length, query_pair.shape[2] * head_size)
    )
    grad_kv = jnp.stack([grad_low, grad_high])
    grad_keys = (grad_kv[:, :, :head_size] * factor).astype(jnp.bfloat16)
    grad_values = grad_kv[:, :, head_size:].astype(jnp.bfloat16)

    def restore(paired):
        return jnp.concatenate([paired[first_slot], paired[second_slot]], 0)

    return (restore(grad_query), restore(grad_keys), restore(grad_values))


def solution(mesh):
    in_specs = (
        P(AXES, None),
        P(AXES, None),
        P(AXES, None),
        P(AXES, None),
        P(),
        P(),
    )
    out_specs = (
        P(AXES, None),
        P(AXES, None),
        P(AXES, None),
    )
    return jax.shard_map(
        on_device, mesh=mesh, in_specs=in_specs, out_specs=out_specs, check_vma=False
    )
```

```python
import math

import jax
import jax.numpy as jnp
from jax import lax
from jax.sharding import PartitionSpec as P


REACH = 6

NEGATIVE = -1e30

AXES = ("outer", "inner")


def fold_source(r, j):
    if j <= r:
        return ("high", j)
    gap = 2 * r + 1 - j
    if gap > 0:
        return ("above", gap)
    if gap == 0:
        return ("own", 0)
    return ("below", -gap)


def on_device(queries, key_states, value_states, grad_output, documents, block_order):
    count = lax.axis_size(AXES)
    device = lax.axis_index(AXES)
    length = key_states.shape[0] // 2
    head_size = key_states.shape[1]
    factor = 1.0 / math.sqrt(head_size)
    span = REACH + 1

    first_slot = jnp.where(block_order[2 * device] < count, 0, 1).astype(jnp.int32)
    second_slot = 1 - first_slot

    def take_block(rows, slot):
        return lax.dynamic_slice_in_dim(rows, slot * length, length, 0)

    joined = jnp.concatenate([key_states, value_states], 1)
    low = take_block(joined, first_slot)
    high = take_block(joined, second_slot)
    odd = (device % 2) == 1
    own = jnp.stack([low, high])
    mate = lax.ppermute(own, AXES, [(s, s ^ 1) for s in range(count)])
    even_part = jnp.where(odd, mate, own)
    odd_part = jnp.where(odd, own, mate)
    chip = jnp.stack([even_part[0], odd_part[0], even_part[1], odd_part[1]])
    lows = {0: chip[0], 1: chip[1]}
    highs = {0: chip[2], 1: chip[3]}
    for j in range(1, REACH // 2 + 1):
        up = [(s, s + 2 * j) for s in range(count - 2 * j)]
        down = [(s, s - 2 * j) for s in range(2 * j, count)]
        below_chip = lax.ppermute(chip[:2], AXES, up)
        above_chip = lax.ppermute(chip, AXES, down)
        lows[-2 * j], lows[1 - 2 * j] = below_chip[0], below_chip[1]
        lows[2 * j], lows[2 * j + 1] = above_chip[0], above_chip[1]
        highs[2 * j], highs[2 * j + 1] = above_chip[2], above_chip[3]

    def by_parity(table, t):
        return jnp.where(odd, table[t + 1], table[t])

    low_window = jnp.concatenate([by_parity(lows, t) for t in range(-REACH, 1)], 0)

    fold_index = jnp.clip(count - 1 - device, 0, REACH)

    def fold_block(r, j):
        parity = (count - 1 - r) % 2
        kind, at = fold_source(r, j)
        return lows[parity + {"above": at, "own": 0, "below": -at}[kind]]

    pieces = []
    for j in range(REACH, 0, -1):
        block = by_parity(highs, j)
        for r in range(j - 1, -1, -1):
            block = jnp.where(fold_index == r, fold_block(r, j), block)
        pieces.append(block)
    high_window = jnp.concatenate(pieces + [by_parity(highs, 0)], 0)
    windows = jnp.stack([low_window, high_window])
    key_window = windows[..., :head_size]
    value_window = windows[..., head_size:]

    def split_heads(rows):
        return rows.reshape(rows.shape[0], rows.shape[1] // head_size, head_size)

    query_pair = jnp.stack(
        [split_heads(take_block(queries, first_slot)), split_heads(take_block(queries, second_slot))]
    )
    output_pair = jnp.stack(
        [
            split_heads(take_block(grad_output, first_slot)),
            split_heads(take_block(grad_output, second_slot)),
        ]
    )

    pad = REACH * length
    padded_documents = jnp.concatenate([jnp.full((pad,), -1, documents.dtype), documents])
    query_blocks = (device, 2 * count - 1 - device)
    offsets = jnp.arange(length, dtype=jnp.int32)
    window_offsets = jnp.arange(span * length, dtype=jnp.int32)
    query_place = jnp.stack([b * length + offsets for b in query_blocks])
    key_place = jnp.stack([b * length - pad + window_offsets for b in query_blocks])
    query_owner = jnp.stack(
        [lax.dynamic_slice_in_dim(documents, b * length, length) for b in query_blocks]
    )
    key_owner = jnp.stack(
        [lax.dynamic_slice_in_dim(padded_documents, b * length, span * length) for b in query_blocks]
    )
    allowed = (
        (key_place[:, None, :] >= 0)
        & (key_place[:, None, :] <= query_place[:, :, None])
        & (key_owner[:, None, :] == query_owner[:, :, None])
    )[:, None]

    scores = (
        jnp.einsum("qbhd,qwd->qhbw", query_pair, key_window, preferred_element_type=jnp.float32)
        * factor
    )
    grad_prob = jnp.einsum(
        "qbhd,qwd->qhbw", output_pair, value_window, preferred_element_type=jnp.float32
    )
    masked = jnp.where(allowed, scores, NEGATIVE)
    top = masked.max(-1)
    weights = jnp.where(allowed, jnp.exp(scores - top[..., None]), 0.0)
    log_totals = top + jnp.log(weights.sum(-1))
    probabilities = jnp.where(allowed, jnp.exp(scores - log_totals[..., None]), 0.0)
    row_dots = (probabilities * grad_prob).sum(-1)
    grad_scores = probabilities * (grad_prob - row_dots[..., None])
    rounded_probs = probabilities.astype(jnp.bfloat16)
    rounded_grads = grad_scores.astype(jnp.bfloat16)

    grad_query = jnp.einsum(
        "qhbw,qwd->qbhd", rounded_grads, key_window, preferred_element_type=jnp.float32
    )
    grad_key = jnp.einsum(
        "qhbw,qbhd->qwd", rounded_grads, query_pair, preferred_element_type=jnp.float32
    )
    grad_value = jnp.einsum(
        "qhbw,qbhd->qwd", rounded_probs, output_pair, preferred_element_type=jnp.float32
    )
    parts = jnp.concatenate([grad_key, grad_value], -1).reshape(2, span, length, 2 * head_size)
    low_parts = parts[0]
    high_parts = parts[1]

    zero = jnp.zeros_like(high_parts[0])
    routed = {}
    for r in range(REACH):
        for j in range(r + 1, REACH + 1):
            routed.setdefault(fold_source(r, j), []).append((r, j))

    def routed_to(kind, at):
        block = zero
        for r, j in routed.get((kind, at), []):
            block = jnp.where(fold_index == r, high_parts[REACH - j], block)
        return block

    to_high = [jnp.where(fold_index >= j, high_parts[REACH - j], zero) for j in range(1, REACH + 1)]
    to_above_low = [routed_to("above", m) for m in range(1, REACH + 1)]
    to_below = [routed_to("below", m) for m in range(1, REACH + 1)]
    to_own_low = routed_to("own", 0)

    grad_low = low_parts[REACH] + to_own_low
    grad_high = high_parts[REACH]
    for k in range(1, REACH + 1):
        up = [(s + k, s) for s in range(count - k)]
        down = [(s - k, s) for s in range(k, count)]
        sent_low = lax.ppermute(low_parts[REACH - k] + to_below[k - 1], AXES, up)
        back = lax.ppermute(jnp.concatenate([to_above_low[k - 1], to_high[k - 1]], 0), AXES, down)
        grad_low = grad_low + sent_low
        grad_low = grad_low + back[:length]
        grad_high = grad_high + back[length:]

    grad_query = (
        (grad_query * factor)
        .astype(jnp.bfloat16)
        .reshape(2, length, query_pair.shape[2] * head_size)
    )
    grad_kv = jnp.stack([grad_low, grad_high])
    grad_keys = (grad_kv[:, :, :head_size] * factor).astype(jnp.bfloat16)
    grad_values = grad_kv[:, :, head_size:].astype(jnp.bfloat16)

    def restore(paired):
        return jnp.concatenate([paired[first_slot], paired[second_slot]], 0)

    return (restore(grad_query), restore(grad_keys), restore(grad_values))


def solution(mesh):
    in_specs = (
        P(AXES, None),
        P(AXES, None),
        P(AXES, None),
        P(AXES, None),
        P(),
        P(),
    )
    out_specs = (
        P(AXES, None),
        P(AXES, None),
        P(AXES, None),
    )

    return jax.shard_map(on_device, mesh=mesh, in_specs=in_specs, out_specs=out_specs, check_vma=False)
```

```python
import math

import jax
import jax.numpy as jnp
from jax import lax
from jax.sharding import PartitionSpec as P


REACH = 6

NEGATIVE = -1e30

AXES = ("outer", "inner")


def fold_source(r, j):
    if j <= r:
        return ("high", j)
    gap = 2 * r + 1 - j
    if gap > 0:
        return ("above", gap)
    if gap == 0:
        return ("own", 0)
    return ("below", -gap)


def on_device(queries, key_states, value_states, grad_output, documents, block_order):
    count = lax.axis_size(AXES)
    device = lax.axis_index(AXES)
    length = key_states.shape[0] // 2
    head_size = key_states.shape[1]
    factor = 1.0 / math.sqrt(head_size)
    span = REACH + 1

    first_slot = jnp.where(block_order[2 * device] < count, 0, 1).astype(jnp.int32)

    swapped = first_slot == 1

    def in_sequence_order(rows):
        paired = rows.reshape((2, length) + rows.shape[1:])
        return jnp.where(swapped, paired[::-1], paired)

    own = in_sequence_order(jnp.concatenate([key_states, value_states], 1))
    odd = (device % 2) == 1
    mate = lax.ppermute(own, AXES, [(s, s ^ 1) for s in range(count)])
    even_part = jnp.where(odd, mate, own)
    odd_part = jnp.where(odd, own, mate)
    chip = jnp.stack([even_part[0], odd_part[0], even_part[1], odd_part[1]])
    lows = {0: chip[0], 1: chip[1]}
    highs = {0: chip[2], 1: chip[3]}
    for j in range(1, REACH // 2 + 1):
        up = [(s, s + 2 * j) for s in range(count - 2 * j)]
        down = [(s, s - 2 * j) for s in range(2 * j, count)]
        below_chip = lax.ppermute(chip[:2], AXES, up)
        above_chip = lax.ppermute(chip, AXES, down)
        lows[-2 * j], lows[1 - 2 * j] = below_chip[0], below_chip[1]
        lows[2 * j], lows[2 * j + 1] = above_chip[0], above_chip[1]
        highs[2 * j], highs[2 * j + 1] = above_chip[2], above_chip[3]

    def by_parity(table, t):
        return jnp.where(odd, table[t + 1], table[t])

    low_window = jnp.concatenate([by_parity(lows, t) for t in range(-REACH, 1)], 0)

    fold_index = jnp.clip(count - 1 - device, 0, REACH)

    def fold_block(r, j):
        parity = (count - 1 - r) % 2
        kind, at = fold_source(r, j)
        return lows[parity + {"above": at, "own": 0, "below": -at}[kind]]

    pieces = []
    for j in range(REACH, 0, -1):
        block = by_parity(highs, j)
        for r in range(j - 1, -1, -1):
            block = jnp.where(fold_index == r, fold_block(r, j), block)
        pieces.append(block)
    high_window = jnp.concatenate(pieces + [by_parity(highs, 0)], 0)
    windows = jnp.stack([low_window, high_window])
    key_window = windows[..., :head_size]
    value_window = windows[..., head_size:]

    heads = queries.shape[1] // head_size
    query_pair = in_sequence_order(queries).reshape(2, length, heads, head_size)
    output_pair = in_sequence_order(grad_output).reshape(2, length, heads, head_size)

    pad = REACH * length
    padded_documents = jnp.concatenate([jnp.full((pad,), -1, documents.dtype), documents])
    query_blocks = (device, 2 * count - 1 - device)
    offsets = jnp.arange(length, dtype=jnp.int32)
    window_offsets = jnp.arange(span * length, dtype=jnp.int32)
    query_place = jnp.stack([b * length + offsets for b in query_blocks])
    key_place = jnp.stack([b * length - pad + window_offsets for b in query_blocks])
    query_owner = jnp.stack(
        [lax.dynamic_slice_in_dim(documents, b * length, length) for b in query_blocks]
    )
    key_owner = jnp.stack(
        [lax.dynamic_slice_in_dim(padded_documents, b * length, span * length) for b in query_blocks]
    )
    allowed = (
        (key_place[:, None, :] >= 0)
        & (key_place[:, None, :] <= query_place[:, :, None])
        & (key_owner[:, None, :] == query_owner[:, :, None])
    )[:, None]

    scores = (
        jnp.einsum("qbhd,qwd->qhbw", query_pair, key_window, preferred_element_type=jnp.float32)
        * factor
    )
    grad_prob = jnp.einsum(
        "qbhd,qwd->qhbw", output_pair, value_window, preferred_element_type=jnp.float32
    )
    masked = jnp.where(allowed, scores, NEGATIVE)
    top = masked.max(-1)
    weights = jnp.where(allowed, jnp.exp(scores - top[..., None]), 0.0)
    log_totals = top + jnp.log(weights.sum(-1))
    probabilities = jnp.where(allowed, jnp.exp(scores - log_totals[..., None]), 0.0)
    row_dots = (probabilities * grad_prob).sum(-1)
    grad_scores = probabilities * (grad_prob - row_dots[..., None])
    rounded_probs = probabilities.astype(jnp.bfloat16)
    rounded_grads = grad_scores.astype(jnp.bfloat16)

    grad_query = jnp.einsum(
        "qhbw,qwd->qbhd", rounded_grads, key_window, preferred_element_type=jnp.float32
    )
    grad_key = jnp.einsum(
        "qhbw,qbhd->qwd", rounded_grads, query_pair, preferred_element_type=jnp.float32
    )
    grad_value = jnp.einsum(
        "qhbw,qbhd->qwd", rounded_probs, output_pair, preferred_element_type=jnp.float32
    )
    parts = jnp.concatenate([grad_key, grad_value], -1).reshape(2, span, length, 2 * head_size)
    low_parts = parts[0]
    high_parts = parts[1]

    zero = jnp.zeros_like(high_parts[0])
    routed = {}
    for r in range(REACH):
        for j in range(r + 1, REACH + 1):
            routed.setdefault(fold_source(r, j), []).append((r, j))

    def routed_to(kind, at):
        block = zero
        for r, j in routed.get((kind, at), []):
            block = jnp.where(fold_index == r, high_parts[REACH - j], block)
        return block

    to_high = [jnp.where(fold_index >= j, high_parts[REACH - j], zero) for j in range(1, REACH + 1)]
    to_above_low = [routed_to("above", m) for m in range(1, REACH + 1)]
    to_below = [routed_to("below", m) for m in range(1, REACH + 1)]
    to_own_low = routed_to("own", 0)

    grad_low = low_parts[REACH] + to_own_low
    grad_high = high_parts[REACH]
    for k in range(1, REACH + 1):
        up = [(s + k, s) for s in range(count - k)]
        down = [(s - k, s) for s in range(k, count)]
        sent_low = lax.ppermute(low_parts[REACH - k] + to_below[k - 1], AXES, up)
        back = lax.ppermute(jnp.concatenate([to_above_low[k - 1], to_high[k - 1]], 0), AXES, down)
        grad_low = grad_low + sent_low
        grad_low = grad_low + back[:length]
        grad_high = grad_high + back[length:]

    grad_query = (
        (grad_query * factor)
        .astype(jnp.bfloat16)
        .reshape(2, length, query_pair.shape[2] * head_size)
    )
    grad_kv = jnp.stack([grad_low, grad_high])
    grad_keys = (grad_kv[:, :, :head_size] * factor).astype(jnp.bfloat16)
    grad_values = grad_kv[:, :, head_size:].astype(jnp.bfloat16)

    def restore(paired):
        return jnp.where(swapped, paired[::-1], paired).reshape((2 * length,) + paired.shape[2:])

    return (restore(grad_query), restore(grad_keys), restore(grad_values))


def solution(mesh):
    in_specs = (
        P(AXES, None),
        P(AXES, None),
        P(AXES, None),
        P(AXES, None),
        P(),
        P(),
    )
    out_specs = (
        P(AXES, None),
        P(AXES, None),
        P(AXES, None),
    )

    return jax.shard_map(on_device, mesh=mesh, in_specs=in_specs, out_specs=out_specs, check_vma=False)
```

```python
import math

import jax
import jax.numpy as jnp
from jax import lax
from jax.sharding import PartitionSpec as P


REACH = 6

NEGATIVE = -1e30

AXES = ("outer", "inner")


def fold_source(r, j):
    if j <= r:
        return ("high", j)
    gap = 2 * r + 1 - j
    if gap > 0:
        return ("above", gap)
    if gap == 0:
        return ("own", 0)
    return ("below", -gap)


def on_device(queries, key_states, value_states, grad_output, documents, block_order):
    count = lax.axis_size(AXES)
    device = lax.axis_index(AXES)
    length = key_states.shape[0] // 2
    head_size = key_states.shape[1]
    factor = 1.0 / math.sqrt(head_size)
    span = REACH + 1

    first_slot = jnp.where(block_order[2 * device] < count, 0, 1).astype(jnp.int32)

    swapped = first_slot == 1

    def in_sequence_order(rows):
        paired = rows.reshape((2, length) + rows.shape[1:])
        return jnp.where(swapped, paired[::-1], paired)

    own = in_sequence_order(jnp.concatenate([key_states, value_states], 1))
    odd = (device % 2) == 1
    mate = lax.ppermute(own, AXES, [(s, s ^ 1) for s in range(count)])
    even_part = jnp.where(odd, mate, own)
    odd_part = jnp.where(odd, own, mate)
    chip = jnp.stack([even_part[0], odd_part[0], even_part[1], odd_part[1]])
    lows = {0: chip[0], 1: chip[1]}
    highs = {0: chip[2], 1: chip[3]}
    fold_lows = set()
    for r in range(REACH):
        for j in range(r + 1, REACH + 1):
            kind, at = fold_source(r, j)
            fold_lows.add((count - 1 - r) % 2 + {"above": at, "own": 0, "below": -at}[kind])
    for j in range(1, REACH // 2 + 1):
        up = [(s, s + 2 * j) for s in range(count - 2 * j)]
        down = [(s, s - 2 * j) for s in range(2 * j, count)]
        below_chip = lax.ppermute(chip[:2], AXES, up)
        lows[-2 * j], lows[1 - 2 * j] = below_chip[0], below_chip[1]
        if fold_lows & {2 * j, 2 * j + 1}:
            above_chip = lax.ppermute(chip, AXES, down)
        else:
            above_chip = lax.ppermute(chip[2:], AXES, down)
        if fold_lows & {2 * j, 2 * j + 1}:
            lows[2 * j], lows[2 * j + 1] = above_chip[0], above_chip[1]
            highs[2 * j], highs[2 * j + 1] = above_chip[2], above_chip[3]
        else:
            highs[2 * j], highs[2 * j + 1] = above_chip[0], above_chip[1]

    def by_parity(table, t):
        return jnp.where(odd, table[t + 1], table[t])

    low_window = jnp.concatenate([by_parity(lows, t) for t in range(-REACH, 1)], 0)

    fold_index = jnp.clip(count - 1 - device, 0, REACH)

    def fold_block(r, j):
        parity = (count - 1 - r) % 2
        kind, at = fold_source(r, j)
        return lows[parity + {"above": at, "own": 0, "below": -at}[kind]]

    pieces = []
    for j in range(REACH, 0, -1):
        block = by_parity(highs, j)
        for r in range(j - 1, -1, -1):
            block = jnp.where(fold_index == r, fold_block(r, j), block)
        pieces.append(block)
    high_window = jnp.concatenate(pieces + [by_parity(highs, 0)], 0)
    windows = jnp.stack([low_window, high_window])
    key_window = windows[..., :head_size]
    value_window = windows[..., head_size:]

    heads = queries.shape[1] // head_size
    query_pair = in_sequence_order(queries).reshape(2, length, heads, head_size)
    output_pair = in_sequence_order(grad_output).reshape(2, length, heads, head_size)

    pad = REACH * length
    padded_documents = jnp.concatenate([jnp.full((pad,), -1, documents.dtype), documents])
    query_blocks = (device, 2 * count - 1 - device)
    offsets = jnp.arange(length, dtype=jnp.int32)
    window_offsets = jnp.arange(span * length, dtype=jnp.int32)
    query_place = jnp.stack([b * length + offsets for b in query_blocks])
    key_place = jnp.stack([b * length - pad + window_offsets for b in query_blocks])
    query_owner = jnp.stack(
        [lax.dynamic_slice_in_dim(documents, b * length, length) for b in query_blocks]
    )
    key_owner = jnp.stack(
        [lax.dynamic_slice_in_dim(padded_documents, b * length, span * length) for b in query_blocks]
    )
    allowed = (
        (key_place[:, None, :] >= 0)
        & (key_place[:, None, :] <= query_place[:, :, None])
        & (key_owner[:, None, :] == query_owner[:, :, None])
    )[:, None]

    scores = (
        jnp.einsum("qbhd,qwd->qhbw", query_pair, key_window, preferred_element_type=jnp.float32)
        * factor
    )
    grad_prob = jnp.einsum(
        "qbhd,qwd->qhbw", output_pair, value_window, preferred_element_type=jnp.float32
    )
    masked = jnp.where(allowed, scores, NEGATIVE)
    top = masked.max(-1)
    weights = jnp.where(allowed, jnp.exp(scores - top[..., None]), 0.0)
    log_totals = top + jnp.log(weights.sum(-1))
    probabilities = jnp.where(allowed, jnp.exp(scores - log_totals[..., None]), 0.0)
    row_dots = (probabilities * grad_prob).sum(-1)
    grad_scores = probabilities * (grad_prob - row_dots[..., None])
    rounded_probs = probabilities.astype(jnp.bfloat16)
    rounded_grads = grad_scores.astype(jnp.bfloat16)

    grad_query = jnp.einsum(
        "qhbw,qwd->qbhd", rounded_grads, key_window, preferred_element_type=jnp.float32
    )
    grad_key = jnp.einsum(
        "qhbw,qbhd->qwd", rounded_grads, query_pair, preferred_element_type=jnp.float32
    )
    grad_value = jnp.einsum(
        "qhbw,qbhd->qwd", rounded_probs, output_pair, preferred_element_type=jnp.float32
    )
    parts = jnp.concatenate([grad_key, grad_value], -1).reshape(2, span, length, 2 * head_size)
    low_parts = parts[0]
    high_parts = parts[1]

    zero = jnp.zeros_like(high_parts[0])
    routed = {}
    for r in range(REACH):
        for j in range(r + 1, REACH + 1):
            routed.setdefault(fold_source(r, j), []).append((r, j))

    def routed_to(kind, at):
        block = zero
        for r, j in routed.get((kind, at), []):
            block = jnp.where(fold_index == r, high_parts[REACH - j], block)
        return block

    to_high = [jnp.where(fold_index >= j, high_parts[REACH - j], zero) for j in range(1, REACH + 1)]
    to_above_low = [routed_to("above", m) for m in range(1, REACH + 1)]
    to_below = [routed_to("below", m) for m in range(1, REACH + 1)]
    to_own_low = routed_to("own", 0)

    grad_low = low_parts[REACH] + to_own_low
    grad_high = high_parts[REACH]
    for k in range(1, REACH + 1):
        up = [(s + k, s) for s in range(count - k)]
        down = [(s - k, s) for s in range(k, count)]
        sent_low = lax.ppermute(low_parts[REACH - k] + to_below[k - 1], AXES, up)
        if ("above", k) in routed:
            back = lax.ppermute(
                jnp.concatenate([to_above_low[k - 1], to_high[k - 1]], 0), AXES, down
            )
        else:
            back = lax.ppermute(to_high[k - 1], AXES, down)
        grad_low = grad_low + sent_low
        if ("above", k) in routed:
            grad_low = grad_low + back[:length]
            back = back[length:]
        grad_high = grad_high + back

    grad_query = (
        (grad_query * factor)
        .astype(jnp.bfloat16)
        .reshape(2, length, query_pair.shape[2] * head_size)
    )
    grad_kv = jnp.stack([grad_low, grad_high])
    grad_keys = (grad_kv[:, :, :head_size] * factor).astype(jnp.bfloat16)
    grad_values = grad_kv[:, :, head_size:].astype(jnp.bfloat16)

    def restore(paired):
        return jnp.where(swapped, paired[::-1], paired).reshape((2 * length,) + paired.shape[2:])

    return (restore(grad_query), restore(grad_keys), restore(grad_values))


def solution(mesh):
    in_specs = (
        P(AXES, None),
        P(AXES, None),
        P(AXES, None),
        P(AXES, None),
        P(),
        P(),
    )
    out_specs = (
        P(AXES, None),
        P(AXES, None),
        P(AXES, None),
    )

    return jax.shard_map(on_device, mesh=mesh, in_specs=in_specs, out_specs=out_specs, check_vma=False)
```

```python
import math

import jax
import jax.numpy as jnp
from jax import lax
from jax.sharding import PartitionSpec as P


REACH = 6

NEGATIVE = -1e30

AXES = ("outer", "inner")


def fold_source(r, j):
    if j <= r:
        return ("high", j)
    gap = 2 * r + 1 - j
    if gap > 0:
        return ("above", gap)
    if gap == 0:
        return ("own", 0)
    return ("below", -gap)


def on_device(queries, key_states, value_states, grad_output, documents, block_order):
    count = lax.axis_size(AXES)
    device = lax.axis_index(AXES)
    length = key_states.shape[0] // 2
    head_size = key_states.shape[1]
    factor = 1.0 / math.sqrt(head_size)
    span = REACH + 1

    first_slot = jnp.where(block_order[2 * device] < count, 0, 1).astype(jnp.int32)

    swapped = first_slot == 1

    def in_sequence_order(rows):
        paired = rows.reshape((2, length) + rows.shape[1:])
        return jnp.where(swapped, paired[::-1], paired)

    stored = jnp.concatenate([key_states, value_states], 1).reshape(2, length, 2 * head_size)
    stored_mate = lax.ppermute(stored, AXES, [(s, s ^ 1) for s in range(count)])
    own = jnp.where(swapped, stored[::-1], stored)
    odd = (device % 2) == 1
    mate_swapped = block_order[2 * (device ^ 1)] >= count
    mate = jnp.where(mate_swapped, stored_mate[::-1], stored_mate)
    even_part = jnp.where(odd, mate, own)
    odd_part = jnp.where(odd, own, mate)
    chip = jnp.stack([even_part[0], odd_part[0], even_part[1], odd_part[1]])
    lows = {0: chip[0], 1: chip[1]}
    highs = {0: chip[2], 1: chip[3]}
    fold_lows = set()
    for r in range(REACH):
        for j in range(r + 1, REACH + 1):
            kind, at = fold_source(r, j)
            fold_lows.add((count - 1 - r) % 2 + {"above": at, "own": 0, "below": -at}[kind])
    for j in range(1, REACH // 2 + 1):
        up = [(s, s + 2 * j) for s in range(count - 2 * j)]
        down = [(s, s - 2 * j) for s in range(2 * j, count)]
        below_chip = lax.ppermute(chip[:2], AXES, up)
        lows[-2 * j], lows[1 - 2 * j] = below_chip[0], below_chip[1]
        if fold_lows & {2 * j, 2 * j + 1}:
            above_chip = lax.ppermute(chip, AXES, down)
        else:
            above_chip = lax.ppermute(chip[2:], AXES, down)
        if fold_lows & {2 * j, 2 * j + 1}:
            lows[2 * j], lows[2 * j + 1] = above_chip[0], above_chip[1]
            highs[2 * j], highs[2 * j + 1] = above_chip[2], above_chip[3]
        else:
            highs[2 * j], highs[2 * j + 1] = above_chip[0], above_chip[1]

    def by_parity(table, t):
        return jnp.where(odd, table[t + 1], table[t])

    low_window = jnp.concatenate([by_parity(lows, t) for t in range(-REACH, 1)], 0)

    fold_index = jnp.clip(count - 1 - device, 0, REACH)

    def fold_block(r, j):
        parity = (count - 1 - r) % 2
        kind, at = fold_source(r, j)
        return lows[parity + {"above": at, "own": 0, "below": -at}[kind]]

    pieces = []
    for j in range(REACH, 0, -1):
        block = by_parity(highs, j)
        for r in range(j - 1, -1, -1):
            block = jnp.where(fold_index == r, fold_block(r, j), block)
        pieces.append(block)
    high_window = jnp.concatenate(pieces + [by_parity(highs, 0)], 0)
    windows = jnp.stack([low_window, high_window])
    key_window = windows[..., :head_size]
    value_window = windows[..., head_size:]

    heads = queries.shape[1] // head_size
    query_pair = in_sequence_order(queries).reshape(2, length, heads, head_size)
    output_pair = in_sequence_order(grad_output).reshape(2, length, heads, head_size)

    pad = REACH * length
    padded_documents = jnp.concatenate([jnp.full((pad,), -1, documents.dtype), documents])
    query_blocks = (device, 2 * count - 1 - device)
    offsets = jnp.arange(length, dtype=jnp.int32)
    window_offsets = jnp.arange(span * length, dtype=jnp.int32)
    query_place = jnp.stack([b * length + offsets for b in query_blocks])
    key_place = jnp.stack([b * length - pad + window_offsets for b in query_blocks])
    query_owner = jnp.stack(
        [lax.dynamic_slice_in_dim(documents, b * length, length) for b in query_blocks]
    )
    key_owner = jnp.stack(
        [lax.dynamic_slice_in_dim(padded_documents, b * length, span * length) for b in query_blocks]
    )
    allowed = (
        (key_place[:, None, :] >= 0)
        & (key_place[:, None, :] <= query_place[:, :, None])
        & (key_owner[:, None, :] == query_owner[:, :, None])
    )[:, None]

    scores = (
        jnp.einsum("qbhd,qwd->qhbw", query_pair, key_window, preferred_element_type=jnp.float32)
        * factor
    )
    grad_prob = jnp.einsum(
        "qbhd,qwd->qhbw", output_pair, value_window, preferred_element_type=jnp.float32
    )
    masked = jnp.where(allowed, scores, NEGATIVE)
    top = masked.max(-1)
    weights = jnp.where(allowed, jnp.exp(scores - top[..., None]), 0.0)
    log_totals = top + jnp.log(weights.sum(-1))
    probabilities = jnp.where(allowed, jnp.exp(scores - log_totals[..., None]), 0.0)
    row_dots = (probabilities * grad_prob).sum(-1)
    grad_scores = probabilities * (grad_prob - row_dots[..., None])
    rounded_probs = probabilities.astype(jnp.bfloat16)
    rounded_grads = grad_scores.astype(jnp.bfloat16)

    grad_query = jnp.einsum(
        "qhbw,qwd->qbhd", rounded_grads, key_window, preferred_element_type=jnp.float32
    )
    grad_key = jnp.einsum(
        "qhbw,qbhd->qwd", rounded_grads, query_pair, preferred_element_type=jnp.float32
    )
    grad_value = jnp.einsum(
        "qhbw,qbhd->qwd", rounded_probs, output_pair, preferred_element_type=jnp.float32
    )
    parts = jnp.concatenate([grad_key, grad_value], -1).reshape(2, span, length, 2 * head_size)
    low_parts = parts[0]
    high_parts = parts[1]

    zero = jnp.zeros_like(high_parts[0])
    routed = {}
    for r in range(REACH):
        for j in range(r + 1, REACH + 1):
            routed.setdefault(fold_source(r, j), []).append((r, j))

    def routed_to(kind, at):
        block = zero
        for r, j in routed.get((kind, at), []):
            block = jnp.where(fold_index == r, high_parts[REACH - j], block)
        return block

    to_high = [jnp.where(fold_index >= j, high_parts[REACH - j], zero) for j in range(1, REACH + 1)]
    to_above_low = [routed_to("above", m) for m in range(1, REACH + 1)]
    to_below = [routed_to("below", m) for m in range(1, REACH + 1)]
    to_own_low = routed_to("own", 0)

    grad_low = low_parts[REACH] + to_own_low
    grad_high = high_parts[REACH]
    received_low = []
    for k in range(1, REACH + 1):
        up = [(s + k, s) for s in range(count - k)]
        down = [(s - k, s) for s in range(k, count)]
        sent_low = lax.ppermute(low_parts[REACH - k] + to_below[k - 1], AXES, up)
        if ("above", k) in routed:
            back = lax.ppermute(
                jnp.concatenate([to_above_low[k - 1], to_high[k - 1]], 0), AXES, down
            )
        else:
            back = lax.ppermute(to_high[k - 1], AXES, down)
        received_low.append(sent_low)
        if ("above", k) in routed:
            grad_low = grad_low + back[:length]
            back = back[length:]
        grad_high = grad_high + back
    grad_low, grad_high = lax.optimization_barrier((grad_low, grad_high))
    for sent_low in received_low:
        grad_low = grad_low + sent_low

    grad_query = (
        (grad_query * factor)
        .astype(jnp.bfloat16)
        .reshape(2, length, query_pair.shape[2] * head_size)
    )
    grad_kv = jnp.stack([grad_low, grad_high])
    grad_keys = (grad_kv[:, :, :head_size] * factor).astype(jnp.bfloat16)
    grad_values = grad_kv[:, :, head_size:].astype(jnp.bfloat16)

    def restore(paired):
        return jnp.where(swapped, paired[::-1], paired).reshape((2 * length,) + paired.shape[2:])

    return (restore(grad_query), restore(grad_keys), restore(grad_values))


def solution(mesh):
    in_specs = (
        P(AXES, None),
        P(AXES, None),
        P(AXES, None),
        P(AXES, None),
        P(),
        P(),
    )
    out_specs = (
        P(AXES, None),
        P(AXES, None),
        P(AXES, None),
    )

    return jax.shard_map(on_device, mesh=mesh, in_specs=in_specs, out_specs=out_specs, check_vma=False)
```
